512 devices in a mesh: dp: 128 (over y, z, core), mp: 4 (over x).
Axes of the slice: x: 4, y: 4, z: 16, core: 2. Of those that a mesh axis runs over, the one named last changes fastest.
Arguments:
- points: float32 [262144, 256], P('dp'), may hold values from -28 to 28
- residual: float32 [128, 262144], P('mp', 'dp'), may hold values from -6 to 6
- coeffs: float32 [128, 262144], P('mp', 'dp'), may hold values from -4 to 4
- block_index: int32 [512], replicated, may hold values from 0 to 262143, as said below
Outputs:
- new_residual: float32 [128, 262144], P('mp', 'dp')
- new_coeffs: float32 [128, 262144], P('mp', 'dp')
The draws below stay inside these ranges and needn't reach their ends.
Inputs may be any that keep to these rules, and one draw needn't show every extreme that they name: `block_index`: distinct example indices; the 2048 examples of one index of dp hold at most 16 of them, and those of some index hold exactly 16.
All inputs are finite; a program needn't handle non-finite values.
Results may differ from the reference program's by a relative error of at most 0.00018.
Values sent between devices are 32-bit elements; how exact they have to be, the bound alone decides.
No kernel may reach another device: no remote copies, remote signals or barrier semaphores. Data moves between devices by JAX's collectives and lax.ppermute only.
A program may use at most 64 MiB of HBM per device.

```python
import math
import jax
import jax.numpy as jnp
from jax import lax

FEAT = 256
OUTPUTS = 128
BLOCK = 512
ROWS = 2048
EXAMPLES = 262144
MOST = 16


def draw_points(key, part):
    base_key, scale_key = jax.random.split(key, 2)
    position = jnp.arange(EXAMPLES, dtype=jnp.float32) / EXAMPLES
    rising = 1.0 + 2.0 * position
    spread = jnp.exp(jax.random.uniform(scale_key, (EXAMPLES, 1), jnp.float32) * math.log(10.0))
    scale = jnp.sqrt(rising[:, None] * spread)
    base = jax.random.truncated_normal(base_key, -5.0, 5.0, (EXAMPLES, FEAT), jnp.float32)
    return (base * scale).astype(jnp.float32)


def draw_block_index(key, part):
    subkeys = jax.random.split(key, 4)
    shard_count = EXAMPLES // ROWS
    others = shard_count - 1
    coordinate = jnp.arange(BLOCK, dtype=jnp.int32)
    remaining = coordinate - MOST
    order_pos = jnp.where(coordinate < MOST, 0, 1 + remaining % others)
    slot_rank = jnp.where(coordinate < MOST, coordinate, remaining // others)
    shuffle = jax.random.permutation(subkeys[0], shard_count).astype(jnp.int32)
    shard_of = shuffle[order_pos]
    offset = jax.random.randint(subkeys[1], (shard_count,), 0, ROWS)
    stride = 2 * jax.random.randint(subkeys[2], (shard_count,), 0, ROWS // 2) + 1
    row_within = (offset[shard_of] + slot_rank * stride[shard_of]) % ROWS
    chosen = shard_of * ROWS + row_within
    reorder = jax.random.permutation(subkeys[3], BLOCK).astype(jnp.int32)
    return chosen[reorder].astype(jnp.int32)


def block_scale(own_key, shape, pieces, low, high):
    def one(dim, shards_of):
        heights = jax.random.uniform(jax.random.fold_in(jax.random.fold_in(own_key, 6), dim), (shards_of,), jnp.float32, low / len(pieces), high / len(pieces))
        return jnp.repeat(jnp.exp(heights), shape[dim] // shards_of).reshape((-1,) + (1,) * (len(shape) - dim - 1))

    loudness = one(*pieces[0])
    for cut in pieces[1:]:
        loudness = loudness * one(*cut)
    return loudness


def centred(stream_key, shape, width, reach, cuts=(), held_as=jnp.bfloat16):
    result = jax.random.normal(stream_key, shape, jnp.float32) * width
    if len(cuts) > 0:
        result = block_scale(stream_key, shape, cuts, -0.22, 0.18) * result
    return jnp.clip(result, min=-reach, max=reach).astype(held_as)


def setup_inputs(seed: int = 0) -> dict:
    key_list = jax.random.split(jax.random.key(seed), 5)
    points = draw_points(jax.random.fold_in(key_list[4], 71), 0)
    residual = centred(key_list[1], (OUTPUTS, EXAMPLES), 1.0, 6.0, ((0, 4), (1, 128)), jnp.float32)
    coeffs = centred(key_list[2], (OUTPUTS, EXAMPLES), 0.5, 4.0, ((0, 4), (1, 128)), jnp.float32)
    block_index = draw_block_index(jax.random.fold_in(key_list[4], 71), 0)
    return {"points": points, "residual": residual, "coeffs": coeffs, "block_index": block_index}


ridge_weight = 1.0

def reference(points, residual, coeffs, block_index):
    highest = lax.Precision.HIGHEST
    mean_sq = jnp.sum(points * points) / EXAMPLES
    block_points = points[block_index]
    block_resid = residual[:, block_index]
    block_sq = jnp.sum(block_points * block_points, axis=1)
    inner_block = lax.dot_general(block_points.astype(jnp.float32), block_points.astype(jnp.float32), (((1,), (1,)), ((), ())), precision=highest, preferred_element_type=jnp.float32)
    kernel_block = jnp.exp(-(block_sq[:, None] + block_sq[None, :] - 2.0 * inner_block) / mean_sq)
    system = kernel_block + ridge_weight * jnp.eye(BLOCK, dtype=jnp.float32)
    factor = jnp.linalg.cholesky(system)
    increment = jax.scipy.linalg.cho_solve((factor, True), block_resid.T).T
    shard_count = EXAMPLES // ROWS
    grouped = points.reshape(shard_count, ROWS, FEAT)

    def change_of(group):
        group_sq = jnp.sum(group * group, axis=1)
        inner = lax.dot_general(block_points.astype(jnp.float32), group.astype(jnp.float32), (((1,), (1,)), ((), ())), precision=highest, preferred_element_type=jnp.float32)
        weights = jnp.exp(-(block_sq[:, None] + group_sq[None, :] - 2.0 * inner) / mean_sq)
        return jnp.dot(increment.astype(jnp.float32), weights.astype(jnp.float32), precision=highest, preferred_element_type=jnp.float32)
    changes = lax.map(change_of, grouped)
    change = jnp.transpose(changes, (1, 0, 2)).reshape(OUTPUTS, EXAMPLES)
    new_residual = (residual - change).at[:, block_index].add(-ridge_weight * increment)
    new_coeffs = coeffs.at[:, block_index].add(increment)
    return (new_residual, new_coeffs)
```

```python
import jax
import jax.numpy as jnp
from jax import lax
from jax.sharding import PartitionSpec as P

BLOCK = 512


ridge_weight = 1.0


def on_device(points, residual, coeffs, block_index):
    highest = lax.Precision.HIGHEST
    shard_rows = points.shape[0]
    feature_count = points.shape[1]
    output_rows = residual.shape[0]
    dp_count = lax.axis_size("dp")
    position = lax.axis_index("dp")
    owner_shard = block_index // shard_rows
    local_row = block_index - owner_shard * shard_rows
    mine = owner_shard == position
    safe_row = jnp.where(mine, local_row, 0)
    own_squares = jnp.sum(points * points, axis=1)
    own_total = jnp.sum(own_squares)
    picked_points = jnp.where(mine[:, None], points[safe_row], 0.0)
    picked_resid = jnp.where(mine[:, None], residual[:, safe_row].T, 0.0)
    body = jnp.concatenate([picked_points, picked_resid], axis=1)
    extra = jnp.zeros((8, feature_count + output_rows), jnp.float32).at[0, 0].set(own_total)
    packed = jnp.concatenate([body, extra], axis=0)
    summed = lax.psum(packed, "dp")
    block_points = summed[:BLOCK, :feature_count]
    block_resid = summed[:BLOCK, feature_count:].T
    mean_sq = summed[BLOCK, 0] / (shard_rows * dp_count)
    block_sq = jnp.sum(block_points * block_points, axis=1)
    inner_block = lax.dot_general(
        block_points,
        block_points,
        (((1,), (1,)), ((), ())),
        precision=highest,
        preferred_element_type=jnp.float32,
    )
    kernel_block = jnp.exp(-(block_sq[:, None] + block_sq[None, :] - 2.0 * inner_block) / mean_sq)
    system = kernel_block + ridge_weight * jnp.eye(BLOCK, dtype=jnp.float32)
    factor = jnp.linalg.cholesky(system)
    increment = jax.scipy.linalg.cho_solve((factor, True), block_resid.T).T
    inner = lax.dot_general(
        block_points,
        points,
        (((1,), (1,)), ((), ())),
        precision=highest,
        preferred_element_type=jnp.float32,
    )
    weights = jnp.exp(-(block_sq[:, None] + own_squares[None, :] - 2.0 * inner) / mean_sq)
    change = jnp.dot(increment, weights, precision=highest, preferred_element_type=jnp.float32)
    column = jnp.where(mine, local_row, shard_rows)
    new_residual = (residual - change).at[:, column].add(-ridge_weight * increment, mode="drop")
    new_coeffs = coeffs.at[:, column].add(increment, mode="drop")
    return (new_residual, new_coeffs)


def solution(mesh):
    placed = (P("dp", None), P("mp", "dp"), P("mp", "dp"), P())
    return jax.shard_map(
        on_device,
        mesh=mesh,
        in_specs=placed,
        out_specs=(P("mp", "dp"), P("mp", "dp")),
        check_vma=False,
    )
```

```python
import jax
import jax.numpy as jnp
from jax import lax
from jax.sharding import Mesh
from jax.sharding import PartitionSpec as P

BLOCK = 512
MOST = 16


ridge_weight = 1.0

DP = ("y", "z", "c")


def on_device(points, residual, coeffs, block_index):
    highest = lax.Precision.HIGHEST
    shard_rows = points.shape[0]
    feature_count = points.shape[1]
    output_rows = residual.shape[0]
    y_count = lax.axis_size("y")
    z_count = lax.axis_size("z")
    c_count = lax.axis_size("c")
    dp_count = y_count * z_count * c_count
    position = (lax.axis_index("y") * z_count + lax.axis_index("z")) * c_count + lax.axis_index("c")
    owner_shard = block_index // shard_rows
    local_row = block_index - owner_shard * shard_rows
    mine = owner_shard == position
    own_squares = jnp.sum(points * points, axis=1)
    own_total = jnp.sum(own_squares)
    same_owner = owner_shard[:, None] == owner_shard[None, :]
    earlier = lax.broadcasted_iota(jnp.int32, (BLOCK, BLOCK), 1) < lax.broadcasted_iota(
        jnp.int32, (BLOCK, BLOCK), 0
    )
    slot_rank = jnp.sum((same_owner & earlier).astype(jnp.int32), axis=1)
    pick = mine[None, :] & (slot_rank[None, :] == lax.broadcasted_iota(jnp.int32, (MOST, BLOCK), 0))
    slot_row = jnp.sum(jnp.where(pick, local_row[None, :], 0), axis=1)
    slot_used = jnp.any(pick, axis=1)
    slot_points = jnp.where(slot_used[:, None], points[slot_row], 0.0)
    slot_resid = jnp.where(slot_used[:, None], residual[:, slot_row].T, 0.0)
    body = jnp.concatenate([slot_points, slot_resid], axis=1)
    extra = jnp.zeros((1, feature_count + output_rows), jnp.float32).at[0, 0].set(own_total)
    packed = jnp.concatenate([body, extra], axis=0)
    per_device = MOST + 1
    gathered = lax.all_gather(packed, "c", axis=0, tiled=True)
    gathered = lax.all_gather(gathered, "y", axis=0, tiled=True)
    gathered = lax.all_gather(gathered, "z", axis=0, tiled=True)
    owner_y = owner_shard // (z_count * c_count)
    owner_z = (owner_shard // c_count) % z_count
    owner_c = owner_shard % c_count
    owner_at = (owner_z * y_count + owner_y) * c_count + owner_c
    where_at = owner_at * per_device + slot_rank
    block_rows = gathered[where_at]
    block_points = block_rows[:, :feature_count]
    block_resid = block_rows[:, feature_count:].T
    square_total = jnp.sum(gathered.reshape(dp_count, per_device, -1)[:, MOST, 0])
    mean_sq = square_total / (shard_rows * dp_count)
    block_sq = jnp.sum(block_points * block_points, axis=1)
    inner_block = lax.dot_general(
        block_points,
        block_points,
        (((1,), (1,)), ((), ())),
        precision=highest,
        preferred_element_type=jnp.float32,
    )
    kernel_block = jnp.exp(-(block_sq[:, None] + block_sq[None, :] - 2.0 * inner_block) / mean_sq)
    system = kernel_block + ridge_weight * jnp.eye(BLOCK, dtype=jnp.float32)
    factor = jnp.linalg.cholesky(system)
    increment = jax.scipy.linalg.cho_solve((factor, True), block_resid.T).T
    inner = lax.dot_general(
        block_points,
        points,
        (((1,), (1,)), ((), ())),
        precision=highest,
        preferred_element_type=jnp.float32,
    )
    weights = jnp.exp(-(block_sq[:, None] + own_squares[None, :] - 2.0 * inner) / mean_sq)
    change = jnp.dot(increment, weights, precision=highest, preferred_element_type=jnp.float32)
    column = jnp.where(mine, local_row, shard_rows)
    new_residual = (residual - change).at[:, column].add(-ridge_weight * increment, mode="drop")
    new_coeffs = coeffs.at[:, column].add(increment, mode="drop")
    return (new_residual, new_coeffs)


def solution(mesh):
    dp_parts = (4, mesh.shape["dp"] // 8, 2)
    split = Mesh(mesh.devices.reshape(dp_parts + (mesh.shape["mp"],)), DP + ("mp",))
    placed = (P(DP, None), P("mp", DP), P("mp", DP), P())
    return jax.shard_map(
        on_device,
        mesh=split,
        in_specs=placed,
        out_specs=(P("mp", DP), P("mp", DP)),
        check_vma=False,
    )
```

```python
import jax
import jax.numpy as jnp
from jax import lax
from jax.sharding import Mesh
from jax.sharding import PartitionSpec as P
from jax.experimental import pallas as pl
from jax.experimental.pallas import tpu as pltpu

BLOCK = 512
MOST = 16


ridge_weight = 1.0

DP = ("y", "z", "c")


NB = 128
G = 8


def _dot_nt(a, b):
    return lax.dot_general(a, b, (((1,), (1,)), ((), ())), precision=lax.Precision.HIGHEST,
                           preferred_element_type=jnp.float32)


def _dot_nn(a, b):
    return lax.dot_general(a, b, (((1,), (0,)), ((), ())), precision=lax.Precision.HIGHEST,
                           preferred_element_type=jnp.float32)


def _dot_tn(a, b):
    return lax.dot_general(a, b, (((0,), (0,)), ((), ())), precision=lax.Precision.HIGHEST,
                           preferred_element_type=jnp.float32)


def _solve_kernel(a_ref, r_ref, x_ref, work, up, inv, dg):
    n = a_ref.shape[0]
    blocks = n // NB
    work[...] = a_ref[...]
    eye = (lax.broadcasted_iota(jnp.int32, (NB, NB), 0) == lax.broadcasted_iota(jnp.int32, (NB, NB), 1)).astype(jnp.float32)
    up[...] = jnp.zeros_like(up)
    lane = lax.broadcasted_iota(jnp.int32, (1, NB), 1)
    sub_g = lax.broadcasted_iota(jnp.int32, (G, 1), 0)
    lane_g = lax.broadcasted_iota(jnp.int32, (G, NB), 1)
    for b in range(blocks):
        r0 = b * NB
        dg[:, :NB] = work[r0:r0 + NB, r0:r0 + NB]
        dg[:, NB:] = eye

        def group(t, carry):
            g0 = pl.multiple_of(t * G, G)
            slab = dg[pl.ds(g0, G), :]
            for j in range(G):
                k = g0 + j
                row = slab[j:j + 1, :]
                c = jnp.sum(jnp.where(lane_g == g0 + sub_g, jnp.broadcast_to(row[:, :NB], (G, NB)), 0.0), axis=1, keepdims=True)
                scale = lax.rsqrt(c[j:j + 1, :])
                u = row * scale
                u_diag = jnp.where(lane >= k, u[:, :NB], 0.0)
                u = jnp.concatenate([u_diag, u[:, NB:]], axis=1)
                u_col = jnp.where(sub_g > j, c * scale, 0.0)
                slab = jnp.where(sub_g == j, u, slab - u_col * u)
            strip = dg[...]
            dg[...] = strip - _dot_tn(slab[:, :NB], slab)
            dg[pl.ds(g0, G), :] = slab
            return carry

        lax.fori_loop(0, NB // G, group, 0)
        up[r0:r0 + NB, r0:r0 + NB] = dg[:, :NB]
        inv[b] = dg[:, NB:]
        if b + 1 < blocks:
            panel = _dot_nn(inv[b], work[r0:r0 + NB, r0 + NB:n])
            up[r0:r0 + NB, r0 + NB:n] = panel
            work[r0 + NB:n, r0 + NB:n] -= _dot_tn(panel, panel)
    rhs = r_ref[...]
    z = []
    for b in range(blocks):
        acc = rhs[:, b * NB:(b + 1) * NB]
        for a in range(b):
            acc = acc - _dot_nn(z[a], up[a * NB:(a + 1) * NB, b * NB:(b + 1) * NB])
        z.append(_dot_nt(acc, inv[b]))
    x = [None] * blocks
    for b in reversed(range(blocks)):
        acc = z[b]
        for a in range(b + 1, blocks):
            acc = acc - _dot_nt(x[a], up[b * NB:(b + 1) * NB, a * NB:(a + 1) * NB])
        x[b] = _dot_nn(acc, inv[b])
    x_ref[...] = jnp.concatenate(x, axis=1)


def spd_solve(system, rhs, interpret=False):
    n = system.shape[0]
    return pl.pallas_call(
        _solve_kernel,
        out_shape=jax.ShapeDtypeStruct(rhs.shape, jnp.float32),
        scratch_shapes=[
            pltpu.VMEM((n, n), jnp.float32),
            pltpu.VMEM((n, n), jnp.float32),
            pltpu.VMEM((n // NB, NB, NB), jnp.float32),
            pltpu.VMEM((NB, 2 * NB), jnp.float32),
        ],
        interpret=interpret,
    )(system, rhs)


def on_device(points, residual, coeffs, block_index):
    highest = lax.Precision.HIGHEST
    shard_rows = points.shape[0]
    feature_count = points.shape[1]
    output_rows = residual.shape[0]
    y_count = lax.axis_size("y")
    z_count = lax.axis_size("z")
    c_count = lax.axis_size("c")
    dp_count = y_count * z_count * c_count
    position = (lax.axis_index("y") * z_count + lax.axis_index("z")) * c_count + lax.axis_index("c")
    owner_shard = block_index // shard_rows
    local_row = block_index - owner_shard * shard_rows
    mine = owner_shard == position
    own_squares = jnp.sum(points * points, axis=1)
    own_total = jnp.sum(own_squares)
    same_owner = owner_shard[:, None] == owner_shard[None, :]
    earlier = lax.broadcasted_iota(jnp.int32, (BLOCK, BLOCK), 1) < lax.broadcasted_iota(
        jnp.int32, (BLOCK, BLOCK), 0
    )
    slot_rank = jnp.sum((same_owner & earlier).astype(jnp.int32), axis=1)
    pick = mine[None, :] & (slot_rank[None, :] == lax.broadcasted_iota(jnp.int32, (MOST, BLOCK), 0))
    slot_row = jnp.sum(jnp.where(pick, local_row[None, :], 0), axis=1)
    slot_used = jnp.any(pick, axis=1)
    slot_points = jnp.where(slot_used[:, None], points[slot_row], 0.0)
    slot_resid = jnp.where(slot_used[:, None], residual[:, slot_row].T, 0.0)
    body = jnp.concatenate([slot_points, slot_resid], axis=1)
    extra = jnp.zeros((1, feature_count + output_rows), jnp.float32).at[0, 0].set(own_total)
    packed = jnp.concatenate([body, extra], axis=0)
    per_device = MOST + 1
    gathered = lax.all_gather(packed, "c", axis=0, tiled=True)
    gathered = lax.all_gather(gathered, "y", axis=0, tiled=True)
    gathered = lax.all_gather(gathered, "z", axis=0, tiled=True)
    owner_y = owner_shard // (z_count * c_count)
    owner_z = (owner_shard // c_count) % z_count
    owner_c = owner_shard % c_count
    owner_at = (owner_z * y_count + owner_y) * c_count + owner_c
    where_at = owner_at * per_device + slot_rank
    block_rows = gathered[where_at]
    block_points = block_rows[:, :feature_count]
    block_resid = block_rows[:, feature_count:].T
    square_total = jnp.sum(gathered.reshape(dp_count, per_device, -1)[:, MOST, 0])
    mean_sq = square_total / (shard_rows * dp_count)
    block_sq = jnp.sum(block_points * block_points, axis=1)
    inner_block = lax.dot_general(
        block_points,
        block_points,
        (((1,), (1,)), ((), ())),
        precision=highest,
        preferred_element_type=jnp.float32,
    )
    kernel_block = jnp.exp(-(block_sq[:, None] + block_sq[None, :] - 2.0 * inner_block) / mean_sq)
    system = kernel_block + ridge_weight * jnp.eye(BLOCK, dtype=jnp.float32)
    increment = spd_solve(system, block_resid)
    inner = lax.dot_general(
        block_points,
        points,
        (((1,), (1,)), ((), ())),
        precision=highest,
        preferred_element_type=jnp.float32,
    )
    weights = jnp.exp(-(block_sq[:, None] + own_squares[None, :] - 2.0 * inner) / mean_sq)
    change = jnp.dot(increment, weights, precision=highest, preferred_element_type=jnp.float32)
    column = jnp.where(mine, local_row, shard_rows)
    new_residual = (residual - change).at[:, column].add(-ridge_weight * increment, mode="drop")
    new_coeffs = coeffs.at[:, column].add(increment, mode="drop")
    return (new_residual, new_coeffs)


def solution(mesh):
    dp_parts = (4, mesh.shape["dp"] // 8, 2)
    split = Mesh(mesh.devices.reshape(dp_parts + (mesh.shape["mp"],)), DP + ("mp",))
    placed = (P(DP, None), P("mp", DP), P("mp", DP), P())
    return jax.shard_map(
        on_device,
        mesh=split,
        in_specs=placed,
        out_specs=(P("mp", DP), P("mp", DP)),
        check_vma=False,
    )
```

```python
import jax
import jax.numpy as jnp
from jax import lax
from jax.sharding import Mesh
from jax.sharding import PartitionSpec as P
from jax.experimental import pallas as pl
from jax.experimental.pallas import tpu as pltpu

BLOCK = 512
MOST = 16


ridge_weight = 1.0

DP = ("y", "z", "c")


NB = 128
G = 8


def _dot_nt(a, b):
    return lax.dot_general(a, b, (((1,), (1,)), ((), ())), precision=lax.Precision.HIGHEST,
                           preferred_element_type=jnp.float32)


def _dot_nn(a, b):
    return lax.dot_general(a, b, (((1,), (0,)), ((), ())), precision=lax.Precision.HIGHEST,
                           preferred_element_type=jnp.float32)


def _dot_tn(a, b):
    return lax.dot_general(a, b, (((0,), (0,)), ((), ())), precision=lax.Precision.HIGHEST,
                           preferred_element_type=jnp.float32)


def _solve_kernel(a_ref, r_ref, x_ref, work, up, inv, dg):
    n = a_ref.shape[0]
    blocks = n // NB
    work[...] = a_ref[...]
    eye = (lax.broadcasted_iota(jnp.int32, (NB, NB), 0) == lax.broadcasted_iota(jnp.int32, (NB, NB), 1)).astype(jnp.float32)
    up[...] = jnp.zeros_like(up)
    lane = lax.broadcasted_iota(jnp.int32, (1, NB), 1)
    sub_g = lax.broadcasted_iota(jnp.int32, (G, 1), 0)
    lane_g = lax.broadcasted_iota(jnp.int32, (G, NB), 1)
    for b in range(blocks):
        r0 = b * NB
        dg[:, :NB] = work[r0:r0 + NB, r0:r0 + NB]
        dg[:, NB:] = eye

        def group(t, carry):
            g0 = pl.multiple_of(t * G, G)
            slab = dg[pl.ds(g0, G), :]
            for j in range(G):
                k = g0 + j
                row = slab[j:j + 1, :]
                c = jnp.sum(jnp.where(lane_g == g0 + sub_g, jnp.broadcast_to(row[:, :NB], (G, NB)), 0.0), axis=1, keepdims=True)
                scale = lax.rsqrt(c[j:j + 1, :])
                u = row * scale
                u_diag = jnp.where(lane >= k, u[:, :NB], 0.0)
                u = jnp.concatenate([u_diag, u[:, NB:]], axis=1)
                u_col = jnp.where(sub_g > j, c * scale, 0.0)
                slab = jnp.where(sub_g == j, u, slab - u_col * u)
            strip = dg[...]
            dg[...] = strip - _dot_tn(slab[:, :NB], slab)
            dg[pl.ds(g0, G), :] = slab
            return carry

        lax.fori_loop(0, NB // G, group, 0)
        up[r0:r0 + NB, r0:r0 + NB] = dg[:, :NB]
        inv[b] = dg[:, NB:]
        if b + 1 < blocks:
            panel = _dot_nn(inv[b], work[r0:r0 + NB, r0 + NB:n])
            up[r0:r0 + NB, r0 + NB:n] = panel
            work[r0 + NB:n, r0 + NB:n] -= _dot_tn(panel, panel)
    rhs = r_ref[...]
    z = []
    for b in range(blocks):
        acc = rhs[:, b * NB:(b + 1) * NB]
        for a in range(b):
            acc = acc - _dot_nn(z[a], up[a * NB:(a + 1) * NB, b * NB:(b + 1) * NB])
        z.append(_dot_nt(acc, inv[b]))
    x = [None] * blocks
    for b in reversed(range(blocks)):
        acc = z[b]
        for a in range(b + 1, blocks):
            acc = acc - _dot_nt(x[a], up[b * NB:(b + 1) * NB, a * NB:(a + 1) * NB])
        x[b] = _dot_nn(acc, inv[b])
    x_ref[...] = jnp.concatenate(x, axis=1)


def spd_solve(system, rhs, interpret=False):
    n = system.shape[0]
    return pl.pallas_call(
        _solve_kernel,
        out_shape=jax.ShapeDtypeStruct(rhs.shape, jnp.float32),
        scratch_shapes=[
            pltpu.VMEM((n, n), jnp.float32),
            pltpu.VMEM((n, n), jnp.float32),
            pltpu.VMEM((n // NB, NB, NB), jnp.float32),
            pltpu.VMEM((NB, 2 * NB), jnp.float32),
        ],
        interpret=interpret,
    )(system, rhs)


def on_device(points, residual, coeffs, block_index):
    highest = lax.Precision.HIGHEST
    shard_rows = points.shape[0]
    feature_count = points.shape[1]
    output_rows = residual.shape[0]
    y_count = lax.axis_size("y")
    z_count = lax.axis_size("z")
    c_count = lax.axis_size("c")
    dp_count = y_count * z_count * c_count
    position = (lax.axis_index("y") * z_count + lax.axis_index("z")) * c_count + lax.axis_index("c")
    owner_shard = block_index // shard_rows
    local_row = block_index - owner_shard * shard_rows
    mine = owner_shard == position
    own_squares = jnp.sum(points * points, axis=1)
    own_total = jnp.sum(own_squares)
    same_owner = owner_shard[:, None] == owner_shard[None, :]
    earlier = lax.broadcasted_iota(jnp.int32, (BLOCK, BLOCK), 1) < lax.broadcasted_iota(
        jnp.int32, (BLOCK, BLOCK), 0
    )
    slot_rank = jnp.sum((same_owner & earlier).astype(jnp.int32), axis=1)
    pick = mine[None, :] & (slot_rank[None, :] == lax.broadcasted_iota(jnp.int32, (MOST, BLOCK), 0))
    slot_row = jnp.sum(jnp.where(pick, local_row[None, :], 0), axis=1)
    slot_used = jnp.any(pick, axis=1)
    mp_count = lax.axis_size("mp")
    share = feature_count // mp_count
    slot_points = lax.dynamic_slice_in_dim(points[slot_row], lax.axis_index("mp") * share, share, 1)
    slot_points = jnp.where(slot_used[:, None], slot_points, 0.0)
    slot_resid = jnp.where(slot_used[:, None], residual[:, slot_row].T, 0.0)
    body = jnp.concatenate([slot_points, slot_resid], axis=1)
    extra = jnp.zeros((1, share + output_rows), jnp.float32).at[0, 0].set(own_total)
    packed = jnp.concatenate([body, extra], axis=0)
    per_device = MOST + 1
    gathered = lax.all_gather(packed, "c", axis=0, tiled=True)
    gathered = lax.all_gather(gathered, "y", axis=0, tiled=True)
    gathered = lax.all_gather(gathered, "z", axis=0, tiled=True)
    owner_y = owner_shard // (z_count * c_count)
    owner_z = (owner_shard // c_count) % z_count
    owner_c = owner_shard % c_count
    owner_at = (owner_z * y_count + owner_y) * c_count + owner_c
    where_at = owner_at * per_device + slot_rank
    block_rows = gathered[where_at]
    block_points = lax.all_gather(block_rows[:, :share], "mp", axis=1, tiled=True)
    block_resid = block_rows[:, share:].T
    square_total = jnp.sum(gathered.reshape(dp_count, per_device, -1)[:, MOST, 0])
    mean_sq = square_total / (shard_rows * dp_count)
    block_sq = jnp.sum(block_points * block_points, axis=1)
    inner_block = lax.dot_general(
        block_points,
        block_points,
        (((1,), (1,)), ((), ())),
        precision=highest,
        preferred_element_type=jnp.float32,
    )
    kernel_block = jnp.exp(-(block_sq[:, None] + block_sq[None, :] - 2.0 * inner_block) / mean_sq)
    system = kernel_block + ridge_weight * jnp.eye(BLOCK, dtype=jnp.float32)
    increment = spd_solve(system, block_resid)
    inner = lax.dot_general(
        block_points,
        points,
        (((1,), (1,)), ((), ())),
        precision=highest,
        preferred_element_type=jnp.float32,
    )
    weights = jnp.exp(-(block_sq[:, None] + own_squares[None, :] - 2.0 * inner) / mean_sq)
    change = jnp.dot(increment, weights, precision=highest, preferred_element_type=jnp.float32)
    column = jnp.where(mine, local_row, shard_rows)
    new_residual = (residual - change).at[:, column].add(-ridge_weight * increment, mode="drop")
    new_coeffs = coeffs.at[:, column].add(increment, mode="drop")
    return (new_residual, new_coeffs)


def solution(mesh):
    dp_parts = (4, mesh.shape["dp"] // 8, 2)
    split = Mesh(mesh.devices.reshape(dp_parts + (mesh.shape["mp"],)), DP + ("mp",))
    placed = (P(DP, None), P("mp", DP), P("mp", DP), P())
    return jax.shard_map(
        on_device,
        mesh=split,
        in_specs=placed,
        out_specs=(P("mp", DP), P("mp", DP)),
        check_vma=False,
    )
```

```python
import jax
import jax.numpy as jnp
from jax import lax
from jax.sharding import Mesh
from jax.sharding import PartitionSpec as P
from jax.experimental import pallas as pl
from jax.experimental.pallas import tpu as pltpu

BLOCK = 512
MOST = 16


ridge_weight = 1.0

DP = ("y", "z", "c")


NB = 128
G = 64


def _dot_nt(a, b):
    return lax.dot_general(a, b, (((1,), (1,)), ((), ())), precision=lax.Precision.HIGHEST,
                           preferred_element_type=jnp.float32)


def _dot_nn(a, b):
    return lax.dot_general(a, b, (((1,), (0,)), ((), ())), precision=lax.Precision.HIGHEST,
                           preferred_element_type=jnp.float32)


def _dot_tn(a, b):
    return lax.dot_general(a, b, (((0,), (0,)), ((), ())), precision=lax.Precision.HIGHEST,
                           preferred_element_type=jnp.float32)


def _solve_kernel(a_ref, r_ref, x_ref, work, up, inv, dg):
    n = a_ref.shape[0]
    blocks = n // NB
    work[...] = a_ref[...]
    eye = (lax.broadcasted_iota(jnp.int32, (NB, NB), 0) == lax.broadcasted_iota(jnp.int32, (NB, NB), 1)).astype(jnp.float32)
    up[...] = jnp.zeros_like(up)
    lane = lax.broadcasted_iota(jnp.int32, (1, NB), 1)
    sub_g = lax.broadcasted_iota(jnp.int32, (G, 1), 0)
    lane_g = lax.broadcasted_iota(jnp.int32, (G, NB), 1)
    for b in range(blocks):
        r0 = b * NB
        dg[:, :NB] = work[r0:r0 + NB, r0:r0 + NB]
        dg[:, NB:] = eye

        def group(t, carry):
            g0 = pl.multiple_of(t * G, G)
            slab = dg[pl.ds(g0, G), :]
            for j in range(G):
                k = g0 + j
                row = slab[j:j + 1, :]
                c = jnp.sum(jnp.where(lane_g == g0 + sub_g, jnp.broadcast_to(row[:, :NB], (G, NB)), 0.0), axis=1, keepdims=True)
                scale = lax.rsqrt(c[j:j + 1, :])
                u = row * scale
                u_diag = jnp.where(lane >= k, u[:, :NB], 0.0)
                u = jnp.concatenate([u_diag, u[:, NB:]], axis=1)
                u_col = jnp.where(sub_g > j, c * scale, 0.0)
                slab = jnp.where(sub_g == j, u, slab - u_col * u)
            strip = dg[...]
            dg[...] = strip - _dot_tn(slab[:, :NB], slab)
            dg[pl.ds(g0, G), :] = slab
            return carry

        lax.fori_loop(0, NB // G, group, 0)
        up[r0:r0 + NB, r0:r0 + NB] = dg[:, :NB]
        inv[b] = dg[:, NB:]
        if b + 1 < blocks:
            panel = _dot_nn(inv[b], work[r0:r0 + NB, r0 + NB:n])
            up[r0:r0 + NB, r0 + NB:n] = panel
            work[r0 + NB:n, r0 + NB:n] -= _dot_tn(panel, panel)
    rhs = r_ref[...]
    z = []
    for b in range(blocks):
        acc = rhs[:, b * NB:(b + 1) * NB]
        for a in range(b):
            acc = acc - _dot_nn(z[a], up[a * NB:(a + 1) * NB, b * NB:(b + 1) * NB])
        z.append(_dot_nt(acc, inv[b]))
    x = [None] * blocks
    for b in reversed(range(blocks)):
        acc = z[b]
        for a in range(b + 1, blocks):
            acc = acc - _dot_nt(x[a], up[b * NB:(b + 1) * NB, a * NB:(a + 1) * NB])
        x[b] = _dot_nn(acc, inv[b])
    x_ref[...] = jnp.concatenate(x, axis=1)


def spd_solve(system, rhs, interpret=False):
    n = system.shape[0]
    return pl.pallas_call(
        _solve_kernel,
        out_shape=jax.ShapeDtypeStruct(rhs.shape, jnp.float32),
        scratch_shapes=[
            pltpu.VMEM((n, n), jnp.float32),
            pltpu.VMEM((n, n), jnp.float32),
            pltpu.VMEM((n // NB, NB, NB), jnp.float32),
            pltpu.VMEM((NB, 2 * NB), jnp.float32),
        ],
        interpret=interpret,
    )(system, rhs)


def on_device(points, residual, coeffs, block_index):
    highest = lax.Precision.HIGHEST
    shard_rows = points.shape[0]
    feature_count = points.shape[1]
    output_rows = residual.shape[0]
    y_count = lax.axis_size("y")
    z_count = lax.axis_size("z")
    c_count = lax.axis_size("c")
    dp_count = y_count * z_count * c_count
    position = (lax.axis_index("y") * z_count + lax.axis_index("z")) * c_count + lax.axis_index("c")
    owner_shard = block_index // shard_rows
    local_row = block_index - owner_shard * shard_rows
    mine = owner_shard == position
    own_squares = jnp.sum(points * points, axis=1)
    own_total = jnp.sum(own_squares)
    same_owner = owner_shard[:, None] == owner_shard[None, :]
    earlier = lax.broadcasted_iota(jnp.int32, (BLOCK, BLOCK), 1) < lax.broadcasted_iota(
        jnp.int32, (BLOCK, BLOCK), 0
    )
    slot_rank = jnp.sum((same_owner & earlier).astype(jnp.int32), axis=1)
    pick = mine[None, :] & (slot_rank[None, :] == lax.broadcasted_iota(jnp.int32, (MOST, BLOCK), 0))
    slot_row = jnp.sum(jnp.where(pick, local_row[None, :], 0), axis=1)
    slot_used = jnp.any(pick, axis=1)
    mp_count = lax.axis_size("mp")
    share = feature_count // mp_count
    slot_points = lax.dynamic_slice_in_dim(points[slot_row], lax.axis_index("mp") * share, share, 1)
    slot_points = jnp.where(slot_used[:, None], slot_points, 0.0)
    slot_resid = jnp.where(slot_used[:, None], residual[:, slot_row].T, 0.0)
    body = jnp.concatenate([slot_points, slot_resid], axis=1)
    extra = jnp.zeros((1, share + output_rows), jnp.float32).at[0, 0].set(own_total)
    packed = jnp.concatenate([body, extra], axis=0)
    per_device = MOST + 1
    gathered = lax.all_gather(packed, "c", axis=0, tiled=True)
    gathered = lax.all_gather(gathered, "y", axis=0, tiled=True)
    gathered = lax.all_gather(gathered, "z", axis=0, tiled=True)
    owner_y = owner_shard // (z_count * c_count)
    owner_z = (owner_shard // c_count) % z_count
    owner_c = owner_shard % c_count
    owner_at = (owner_z * y_count + owner_y) * c_count + owner_c
    where_at = owner_at * per_device + slot_rank
    block_rows = gathered[where_at]
    block_points = lax.all_gather(block_rows[:, :share], "mp", axis=1, tiled=True)
    block_resid = block_rows[:, share:].T
    square_total = jnp.sum(gathered.reshape(dp_count, per_device, -1)[:, MOST, 0])
    mean_sq = square_total / (shard_rows * dp_count)
    block_sq = jnp.sum(block_points * block_points, axis=1)
    inner_block = lax.dot_general(
        block_points,
        block_points,
        (((1,), (1,)), ((), ())),
        precision=highest,
        preferred_element_type=jnp.float32,
    )
    kernel_block = jnp.exp(-(block_sq[:, None] + block_sq[None, :] - 2.0 * inner_block) / mean_sq)
    system = kernel_block + ridge_weight * jnp.eye(BLOCK, dtype=jnp.float32)
    increment = spd_solve(system, block_resid)
    inner = lax.dot_general(
        block_points,
        points,
        (((1,), (1,)), ((), ())),
        precision=highest,
        preferred_element_type=jnp.float32,
    )
    weights = jnp.exp(-(block_sq[:, None] + own_squares[None, :] - 2.0 * inner) / mean_sq)
    change = jnp.dot(increment, weights, precision=highest, preferred_element_type=jnp.float32)
    column = jnp.where(mine, local_row, shard_rows)
    new_residual = (residual - change).at[:, column].add(-ridge_weight * increment, mode="drop")
    new_coeffs = coeffs.at[:, column].add(increment, mode="drop")
    return (new_residual, new_coeffs)


def solution(mesh):
    dp_parts = (4, mesh.shape["dp"] // 8, 2)
    split = Mesh(mesh.devices.reshape(dp_parts + (mesh.shape["mp"],)), DP + ("mp",))
    placed = (P(DP, None), P("mp", DP), P("mp", DP), P())
    return jax.shard_map(
        on_device,
        mesh=split,
        in_specs=placed,
        out_specs=(P("mp", DP), P("mp", DP)),
        check_vma=False,
    )
```

```python
import jax
import jax.numpy as jnp
from jax import lax
from jax.sharding import Mesh
from jax.sharding import PartitionSpec as P
from jax.experimental import pallas as pl
from jax.experimental.pallas import tpu as pltpu

BLOCK = 512
MOST = 16


ridge_weight = 1.0

DP = ("y", "z", "c")


NB = 128
G = 64


def _dot_nt(a, b):
    return lax.dot_general(a, b, (((1,), (1,)), ((), ())), precision=lax.Precision.HIGHEST,
                           preferred_element_type=jnp.float32)


def _dot_nn(a, b):
    return lax.dot_general(a, b, (((1,), (0,)), ((), ())), precision=lax.Precision.HIGHEST,
                           preferred_element_type=jnp.float32)


def _dot_tn(a, b):
    return lax.dot_general(a, b, (((0,), (0,)), ((), ())), precision=lax.Precision.HIGHEST,
                           preferred_element_type=jnp.float32)


def _solve_kernel(a_ref, r_ref, x_ref, work, up, inv, dg):
    n = a_ref.shape[0]
    blocks = n // NB
    work[...] = a_ref[...]
    eye = (lax.broadcasted_iota(jnp.int32, (NB, NB), 0) == lax.broadcasted_iota(jnp.int32, (NB, NB), 1)).astype(jnp.float32)
    up[...] = jnp.zeros_like(up)
    lane = lax.broadcasted_iota(jnp.int32, (1, NB), 1)
    sub_g = lax.broadcasted_iota(jnp.int32, (G, 1), 0)
    lane_g = lax.broadcasted_iota(jnp.int32, (G, NB), 1)
    for b in range(blocks):
        r0 = b * NB
        dg[:, :NB] = work[r0:r0 + NB, r0:r0 + NB]
        dg[:, NB:] = eye

        def group(t, carry):
            g0 = pl.multiple_of(t * G, G)
            slab = dg[pl.ds(g0, G), :]
            for j in range(G):
                k = g0 + j
                row = slab[j:j + 1, :]
                c = jnp.sum(jnp.where(lane_g == g0 + sub_g, jnp.broadcast_to(row[:, :NB], (G, NB)), 0.0), axis=1, keepdims=True)
                scale = lax.rsqrt(c[j:j + 1, :])
                u = row * scale
                u_diag = jnp.where(lane >= k, u[:, :NB], 0.0)
                u = jnp.concatenate([u_diag, u[:, NB:]], axis=1)
                u_col = jnp.where(sub_g > j, c * scale, 0.0)
                slab = jnp.where(sub_g == j, u, slab - u_col * u)
            strip = dg[...]
            dg[...] = strip - _dot_tn(slab[:, :NB], slab)
            dg[pl.ds(g0, G), :] = slab
            return carry

        lax.fori_loop(0, NB // G, group, 0)
        up[r0:r0 + NB, r0:r0 + NB] = dg[:, :NB]
        inv[b] = dg[:, NB:]
        if b + 1 < blocks:
            panel = _dot_nn(inv[b], work[r0:r0 + NB, r0 + NB:n])
            up[r0:r0 + NB, r0 + NB:n] = panel
            work[r0 + NB:n, r0 + NB:n] -= _dot_tn(panel, panel)
    rhs = r_ref[...]
    z = []
    for b in range(blocks):
        acc = rhs[:, b * NB:(b + 1) * NB]
        for a in range(b):
            acc = acc - _dot_nn(z[a], up[a * NB:(a + 1) * NB, b * NB:(b + 1) * NB])
        z.append(_dot_nt(acc, inv[b]))
    x = [None] * blocks
    for b in reversed(range(blocks)):
        acc = z[b]
        for a in range(b + 1, blocks):
            acc = acc - _dot_nt(x[a], up[b * NB:(b + 1) * NB, a * NB:(a + 1) * NB])
        x[b] = _dot_nn(acc, inv[b])
    x_ref[...] = jnp.concatenate(x, axis=1)


def spd_solve(system, rhs, interpret=False):
    n = system.shape[0]
    return pl.pallas_call(
        _solve_kernel,
        out_shape=jax.ShapeDtypeStruct(rhs.shape, jnp.float32),
        scratch_shapes=[
            pltpu.VMEM((n, n), jnp.float32),
            pltpu.VMEM((n, n), jnp.float32),
            pltpu.VMEM((n // NB, NB, NB), jnp.float32),
            pltpu.VMEM((NB, 2 * NB), jnp.float32),
        ],
        interpret=interpret,
    )(system, rhs)


def on_device(points, residual, coeffs, block_index):
    highest = lax.Precision.HIGHEST
    shard_rows = points.shape[0]
    feature_count = points.shape[1]
    output_rows = residual.shape[0]
    y_count = lax.axis_size("y")
    z_count = lax.axis_size("z")
    c_count = lax.axis_size("c")
    dp_count = y_count * z_count * c_count
    position = (lax.axis_index("y") * z_count + lax.axis_index("z")) * c_count + lax.axis_index("c")
    owner_shard = block_index // shard_rows
    local_row = block_index - owner_shard * shard_rows
    mine = owner_shard == position
    own_squares = jnp.sum(points * points, axis=1)
    own_total = jnp.sum(own_squares)
    same_owner = owner_shard[:, None] == owner_shard[None, :]
    earlier = lax.broadcasted_iota(jnp.int32, (BLOCK, BLOCK), 1) < lax.broadcasted_iota(
        jnp.int32, (BLOCK, BLOCK), 0
    )
    slot_rank = jnp.sum((same_owner & earlier).astype(jnp.int32), axis=1)
    pick = mine[None, :] & (slot_rank[None, :] == lax.broadcasted_iota(jnp.int32, (MOST, BLOCK), 0))
    slot_row = jnp.sum(jnp.where(pick, local_row[None, :], 0), axis=1)
    slot_used = jnp.any(pick, axis=1)
    mp_count = lax.axis_size("mp")
    share = feature_count // mp_count
    slot_points = lax.dynamic_slice_in_dim(points[slot_row], lax.axis_index("mp") * share, share, 1)
    slot_points = jnp.where(slot_used[:, None], slot_points, 0.0)
    slot_resid = jnp.where(slot_used[:, None], residual[:, slot_row].T, 0.0)
    body = jnp.concatenate([slot_points, slot_resid], axis=1)
    extra = jnp.zeros((1, share + output_rows), jnp.float32).at[0, 0].set(own_total)
    packed = jnp.concatenate([body, extra], axis=0)
    per_device = MOST + 1
    gathered = lax.all_gather(packed, "c", axis=0, tiled=True)
    gathered = lax.all_gather(gathered, "z", axis=0, tiled=True)
    gathered = lax.all_gather(gathered, "y", axis=0, tiled=True)
    where_at = owner_shard * per_device + slot_rank
    block_rows = gathered[where_at]
    block_points = lax.all_gather(block_rows[:, :share], "mp", axis=1, tiled=True)
    block_resid = block_rows[:, share:].T
    square_total = jnp.sum(gathered.reshape(dp_count, per_device, -1)[:, MOST, 0])
    mean_sq = square_total / (shard_rows * dp_count)
    block_sq = jnp.sum(block_points * block_points, axis=1)
    inner_block = lax.dot_general(
        block_points,
        block_points,
        (((1,), (1,)), ((), ())),
        precision=highest,
        preferred_element_type=jnp.float32,
    )
    kernel_block = jnp.exp(-(block_sq[:, None] + block_sq[None, :] - 2.0 * inner_block) / mean_sq)
    system = kernel_block + ridge_weight * jnp.eye(BLOCK, dtype=jnp.float32)
    increment = spd_solve(system, block_resid)
    inner = lax.dot_general(
        block_points,
        points,
        (((1,), (1,)), ((), ())),
        precision=highest,
        preferred_element_type=jnp.float32,
    )
    weights = jnp.exp(-(block_sq[:, None] + own_squares[None, :] - 2.0 * inner) / mean_sq)
    change = jnp.dot(increment, weights, precision=highest, preferred_element_type=jnp.float32)
    column = jnp.where(mine, local_row, shard_rows)
    placed = (column[:, None] == lax.broadcasted_iota(jnp.int32, (BLOCK, shard_rows), 1)).astype(jnp.float32)
    spread = jnp.dot(increment, placed, precision=highest, preferred_element_type=jnp.float32)
    new_residual = (residual - change) - ridge_weight * spread
    new_coeffs = coeffs + spread
    return (new_residual, new_coeffs)


def solution(mesh):
    dp_parts = (4, mesh.shape["dp"] // 8, 2)
    split = Mesh(mesh.devices.reshape(dp_parts + (mesh.shape["mp"],)), DP + ("mp",))
    placed = (P(DP, None), P("mp", DP), P("mp", DP), P())
    return jax.shard_map(
        on_device,
        mesh=split,
        in_specs=placed,
        out_specs=(P("mp", DP), P("mp", DP)),
        check_vma=False,
    )
```

```python
import jax
import jax.numpy as jnp
from jax import lax
from jax.sharding import Mesh
from jax.sharding import PartitionSpec as P
from jax.experimental import pallas as pl
from jax.experimental.pallas import tpu as pltpu

BLOCK = 512
MOST = 16


ridge_weight = 1.0

DP = ("y", "z", "c")


NB = 128
G = 128


def _dot_nt(a, b):
    return lax.dot_general(a, b, (((1,), (1,)), ((), ())), precision=lax.Precision.HIGHEST,
                           preferred_element_type=jnp.float32)


def _dot_nn(a, b):
    return lax.dot_general(a, b, (((1,), (0,)), ((), ())), precision=lax.Precision.HIGHEST,
                           preferred_element_type=jnp.float32)


def _dot_tn(a, b):
    return lax.dot_general(a, b, (((0,), (0,)), ((), ())), precision=lax.Precision.HIGHEST,
                           preferred_element_type=jnp.float32)


def _solve_kernel(a_ref, r_ref, x_ref, work, up, inv, dg):
    n = a_ref.shape[0]
    blocks = n // NB
    work[...] = a_ref[...]
    eye = (lax.broadcasted_iota(jnp.int32, (NB, NB), 0) == lax.broadcasted_iota(jnp.int32, (NB, NB), 1)).astype(jnp.float32)
    up[...] = jnp.zeros_like(up)
    lane = lax.broadcasted_iota(jnp.int32, (1, NB), 1)
    sub_g = lax.broadcasted_iota(jnp.int32, (G, 1), 0)
    lane_g = lax.broadcasted_iota(jnp.int32, (G, NB), 1)
    for b in range(blocks):
        r0 = b * NB
        dg[:, :NB] = work[r0:r0 + NB, r0:r0 + NB]
        dg[:, NB:] = eye

        def group(t, carry):
            g0 = pl.multiple_of(t * G, G)
            slab = dg[pl.ds(g0, G), :]
            for j in range(G):
                k = g0 + j
                row = slab[j:j + 1, :]
                c = jnp.sum(jnp.where(lane_g == g0 + sub_g, jnp.broadcast_to(row[:, :NB], (G, NB)), 0.0), axis=1, keepdims=True)
                scale = lax.rsqrt(c[j:j + 1, :])
                u = row * scale
                u_diag = jnp.where(lane >= k, u[:, :NB], 0.0)
                u = jnp.concatenate([u_diag, u[:, NB:]], axis=1)
                u_col = jnp.where(sub_g > j, c * scale, 0.0)
                slab = jnp.where(sub_g == j, u, slab - u_col * u)
            strip = dg[...]
            dg[...] = strip - _dot_tn(slab[:, :NB], slab)
            dg[pl.ds(g0, G), :] = slab
            return carry

        lax.fori_loop(0, NB // G, group, 0)
        up[r0:r0 + NB, r0:r0 + NB] = dg[:, :NB]
        inv[b] = dg[:, NB:]
        if b + 1 < blocks:
            panel = _dot_nn(inv[b], work[r0:r0 + NB, r0 + NB:n])
            up[r0:r0 + NB, r0 + NB:n] = panel
            work[r0 + NB:n, r0 + NB:n] -= _dot_tn(panel, panel)
    rhs = r_ref[...]
    z = []
    for b in range(blocks):
        acc = rhs[:, b * NB:(b + 1) * NB]
        for a in range(b):
            acc = acc - _dot_nn(z[a], up[a * NB:(a + 1) * NB, b * NB:(b + 1) * NB])
        z.append(_dot_nt(acc, inv[b]))
    x = [None] * blocks
    for b in reversed(range(blocks)):
        acc = z[b]
        for a in range(b + 1, blocks):
            acc = acc - _dot_nt(x[a], up[b * NB:(b + 1) * NB, a * NB:(a + 1) * NB])
        x[b] = _dot_nn(acc, inv[b])
    x_ref[...] = jnp.concatenate(x, axis=1)


def spd_solve(system, rhs, interpret=False):
    n = system.shape[0]
    return pl.pallas_call(
        _solve_kernel,
        out_shape=jax.ShapeDtypeStruct(rhs.shape, jnp.float32),
        scratch_shapes=[
            pltpu.VMEM((n, n), jnp.float32),
            pltpu.VMEM((n, n), jnp.float32),
            pltpu.VMEM((n // NB, NB, NB), jnp.float32),
            pltpu.VMEM((NB, 2 * NB), jnp.float32),
        ],
        interpret=interpret,
    )(system, rhs)


def on_device(points, residual, coeffs, block_index):
    highest = lax.Precision.HIGHEST
    shard_rows = points.shape[0]
    feature_count = points.shape[1]
    output_rows = residual.shape[0]
    y_count = lax.axis_size("y")
    z_count = lax.axis_size("z")
    c_count = lax.axis_size("c")
    dp_count = y_count * z_count * c_count
    position = (lax.axis_index("y") * z_count + lax.axis_index("z")) * c_count + lax.axis_index("c")
    owner_shard = block_index // shard_rows
    local_row = block_index - owner_shard * shard_rows
    mine = owner_shard == position
    own_squares = jnp.sum(points * points, axis=1)
    own_total = jnp.sum(own_squares)
    same_owner = owner_shard[:, None] == owner_shard[None, :]
    earlier = lax.broadcasted_iota(jnp.int32, (BLOCK, BLOCK), 1) < lax.broadcasted_iota(
        jnp.int32, (BLOCK, BLOCK), 0
    )
    slot_rank = jnp.sum((same_owner & earlier).astype(jnp.int32), axis=1)
    pick = mine[None, :] & (slot_rank[None, :] == lax.broadcasted_iota(jnp.int32, (MOST, BLOCK), 0))
    slot_row = jnp.sum(jnp.where(pick, local_row[None, :], 0), axis=1)
    slot_used = jnp.any(pick, axis=1)
    mp_count = lax.axis_size("mp")
    share = feature_count // mp_count
    slot_points = lax.dynamic_slice_in_dim(points[slot_row], lax.axis_index("mp") * share, share, 1)
    slot_points = jnp.where(slot_used[:, None], slot_points, 0.0)
    slot_resid = jnp.where(slot_used[:, None], residual[:, slot_row].T, 0.0)
    body = jnp.concatenate([slot_points, slot_resid], axis=1)
    extra = jnp.zeros((1, share + output_rows), jnp.float32).at[0, 0].set(own_total)
    packed = jnp.concatenate([body, extra], axis=0)
    per_device = MOST + 1
    gathered = lax.all_gather(packed, "c", axis=0, tiled=True)
    gathered = lax.all_gather(gathered, "z", axis=0, tiled=True)
    gathered = lax.all_gather(gathered, "y", axis=0, tiled=True)
    where_at = owner_shard * per_device + slot_rank
    block_rows = gathered[where_at]
    block_points = lax.all_gather(block_rows[:, :share], "mp", axis=1, tiled=True)
    block_resid = block_rows[:, share:].T
    square_total = jnp.sum(gathered.reshape(dp_count, per_device, -1)[:, MOST, 0])
    mean_sq = square_total / (shard_rows * dp_count)
    block_sq = jnp.sum(block_points * block_points, axis=1)
    inner_block = lax.dot_general(
        block_points,
        block_points,
        (((1,), (1,)), ((), ())),
        precision=highest,
        preferred_element_type=jnp.float32,
    )
    kernel_block = jnp.exp(-(block_sq[:, None] + block_sq[None, :] - 2.0 * inner_block) / mean_sq)
    system = kernel_block + ridge_weight * jnp.eye(BLOCK, dtype=jnp.float32)
    increment = spd_solve(system, block_resid)
    inner = lax.dot_general(
        block_points,
        points,
        (((1,), (1,)), ((), ())),
        precision=highest,
        preferred_element_type=jnp.float32,
    )
    weights = jnp.exp(-(block_sq[:, None] + own_squares[None, :] - 2.0 * inner) / mean_sq)
    change = jnp.dot(increment, weights, precision=highest, preferred_element_type=jnp.float32)
    column = jnp.where(mine, local_row, shard_rows)
    placed = (column[:, None] == lax.broadcasted_iota(jnp.int32, (BLOCK, shard_rows), 1)).astype(jnp.float32)
    spread = jnp.dot(increment, placed, precision=highest, preferred_element_type=jnp.float32)
    new_residual = (residual - change) - ridge_weight * spread
    new_coeffs = coeffs + spread
    return (new_residual, new_coeffs)


def solution(mesh):
    dp_parts = (4, mesh.shape["dp"] // 8, 2)
    split = Mesh(mesh.devices.reshape(dp_parts + (mesh.shape["mp"],)), DP + ("mp",))
    placed = (P(DP, None), P("mp", DP), P("mp", DP), P())
    return jax.shard_map(
        on_device,
        mesh=split,
        in_specs=placed,
        out_specs=(P("mp", DP), P("mp", DP)),
        check_vma=False,
    )
```

```python
import jax
import jax.numpy as jnp
from jax import lax
from jax.sharding import Mesh
from jax.sharding import PartitionSpec as P
from jax.experimental import pallas as pl
from jax.experimental.pallas import tpu as pltpu

BLOCK = 512
MOST = 16


ridge_weight = 1.0

DP = ("y", "z", "c")


NB = 128
G = 128


def _dot_nt(a, b):
    return lax.dot_general(a, b, (((1,), (1,)), ((), ())), precision=lax.Precision.HIGHEST,
                           preferred_element_type=jnp.float32)


def _dot_nn(a, b):
    return lax.dot_general(a, b, (((1,), (0,)), ((), ())), precision=lax.Precision.HIGHEST,
                           preferred_element_type=jnp.float32)


def _dot_tn(a, b):
    return lax.dot_general(a, b, (((0,), (0,)), ((), ())), precision=lax.Precision.HIGHEST,
                           preferred_element_type=jnp.float32)


def _solve_kernel(p_ref, sq_col_ref, sq_row_ref, m_ref, r_ref, x_ref, work, up, inv, dg):
    n = p_ref.shape[0]
    blocks = n // NB
    p = p_ref[...]
    inner = _dot_nt(p, p)
    kern = jnp.exp(-(sq_col_ref[...] + sq_row_ref[...] - 2.0 * inner) / m_ref[...])
    on_diag = lax.broadcasted_iota(jnp.int32, (n, n), 0) == lax.broadcasted_iota(jnp.int32, (n, n), 1)
    work[...] = jnp.where(on_diag, kern + ridge_weight, kern)
    eye = (lax.broadcasted_iota(jnp.int32, (NB, NB), 0) == lax.broadcasted_iota(jnp.int32, (NB, NB), 1)).astype(jnp.float32)
    up[...] = jnp.zeros_like(up)
    lane = lax.broadcasted_iota(jnp.int32, (1, NB), 1)
    sub_g = lax.broadcasted_iota(jnp.int32, (G, 1), 0)
    lane_g = lax.broadcasted_iota(jnp.int32, (G, NB), 1)
    for b in range(blocks):
        r0 = b * NB
        dg[:, :NB] = work[r0:r0 + NB, r0:r0 + NB]
        dg[:, NB:] = eye

        def group(t, carry):
            g0 = pl.multiple_of(t * G, G)
            slab = dg[pl.ds(g0, G), :]
            for j in range(G):
                k = g0 + j
                row = slab[j:j + 1, :]
                c = jnp.sum(jnp.where(lane_g == g0 + sub_g, jnp.broadcast_to(row[:, :NB], (G, NB)), 0.0), axis=1, keepdims=True)
                scale = lax.rsqrt(c[j:j + 1, :])
                u = row * scale
                u_diag = jnp.where(lane >= k, u[:, :NB], 0.0)
                u = jnp.concatenate([u_diag, u[:, NB:]], axis=1)
                u_col = jnp.where(sub_g > j, c * scale, 0.0)
                slab = jnp.where(sub_g == j, u, slab - u_col * u)
            strip = dg[...]
            dg[...] = strip - _dot_tn(slab[:, :NB], slab)
            dg[pl.ds(g0, G), :] = slab
            return carry

        lax.fori_loop(0, NB // G, group, 0)
        up[r0:r0 + NB, r0:r0 + NB] = dg[:, :NB]
        inv[b] = dg[:, NB:]
        if b + 1 < blocks:
            panel = _dot_nn(inv[b], work[r0:r0 + NB, r0 + NB:n])
            up[r0:r0 + NB, r0 + NB:n] = panel
            work[r0 + NB:n, r0 + NB:n] -= _dot_tn(panel, panel)
    rhs = r_ref[...]
    z = []
    for b in range(blocks):
        acc = rhs[:, b * NB:(b + 1) * NB]
        for a in range(b):
            acc = acc - _dot_nn(z[a], up[a * NB:(a + 1) * NB, b * NB:(b + 1) * NB])
        z.append(_dot_nt(acc, inv[b]))
    x = [None] * blocks
    for b in reversed(range(blocks)):
        acc = z[b]
        for a in range(b + 1, blocks):
            acc = acc - _dot_nt(x[a], up[b * NB:(b + 1) * NB, a * NB:(a + 1) * NB])
        x[b] = _dot_nn(acc, inv[b])
    x_ref[...] = jnp.concatenate(x, axis=1)


def spd_solve(block_points, block_sq, mean_sq, rhs, interpret=False):
    n = block_points.shape[0]
    return pl.pallas_call(
        _solve_kernel,
        out_shape=jax.ShapeDtypeStruct(rhs.shape, jnp.float32),
        scratch_shapes=[
            pltpu.VMEM((n, n), jnp.float32),
            pltpu.VMEM((n, n), jnp.float32),
            pltpu.VMEM((n // NB, NB, NB), jnp.float32),
            pltpu.VMEM((NB, 2 * NB), jnp.float32),
        ],
        interpret=interpret,
    )(block_points, block_sq[:, None], block_sq[None, :], jnp.reshape(mean_sq, (1, 1)), rhs)


def on_device(points, residual, coeffs, block_index):
    highest = lax.Precision.HIGHEST
    shard_rows = points.shape[0]
    feature_count = points.shape[1]
    output_rows = residual.shape[0]
    y_count = lax.axis_size("y")
    z_count = lax.axis_size("z")
    c_count = lax.axis_size("c")
    dp_count = y_count * z_count * c_count
    position = (lax.axis_index("y") * z_count + lax.axis_index("z")) * c_count + lax.axis_index("c")
    owner_shard = block_index // shard_rows
    local_row = block_index - owner_shard * shard_rows
    mine = owner_shard == position
    own_squares = jnp.sum(points * points, axis=1)
    own_total = jnp.sum(own_squares)
    same_owner = owner_shard[:, None] == owner_shard[None, :]
    earlier = lax.broadcasted_iota(jnp.int32, (BLOCK, BLOCK), 1) < lax.broadcasted_iota(
        jnp.int32, (BLOCK, BLOCK), 0
    )
    slot_rank = jnp.sum((same_owner & earlier).astype(jnp.int32), axis=1)
    pick = mine[None, :] & (slot_rank[None, :] == lax.broadcasted_iota(jnp.int32, (MOST, BLOCK), 0))
    slot_row = jnp.sum(jnp.where(pick, local_row[None, :], 0), axis=1)
    slot_used = jnp.any(pick, axis=1)
    mp_count = lax.axis_size("mp")
    share = feature_count // mp_count
    slot_points = lax.dynamic_slice_in_dim(points[slot_row], lax.axis_index("mp") * share, share, 1)
    slot_points = jnp.where(slot_used[:, None], slot_points, 0.0)
    slot_resid = jnp.where(slot_used[:, None], residual[:, slot_row].T, 0.0)
    body = jnp.concatenate([slot_points, slot_resid], axis=1)
    extra = jnp.zeros((1, share + output_rows), jnp.float32).at[0, 0].set(own_total)
    packed = jnp.concatenate([body, extra], axis=0)
    per_device = MOST + 1
    gathered = lax.all_gather(packed, "c", axis=0, tiled=True)
    gathered = lax.all_gather(gathered, "z", axis=0, tiled=True)
    gathered = lax.all_gather(gathered, "y", axis=0, tiled=True)
    where_at = owner_shard * per_device + slot_rank
    block_rows = gathered[where_at]
    block_points = lax.all_gather(block_rows[:, :share], "mp", axis=1, tiled=True)
    block_resid = block_rows[:, share:].T
    square_total = jnp.sum(gathered.reshape(dp_count, per_device, -1)[:, MOST, 0])
    mean_sq = square_total / (shard_rows * dp_count)
    block_sq = jnp.sum(block_points * block_points, axis=1)
    increment = spd_solve(block_points, block_sq, mean_sq, block_resid)
    inner = lax.dot_general(
        block_points,
        points,
        (((1,), (1,)), ((), ())),
        precision=highest,
        preferred_element_type=jnp.float32,
    )
    weights = jnp.exp(-(block_sq[:, None] + own_squares[None, :] - 2.0 * inner) / mean_sq)
    change = jnp.dot(increment, weights, precision=highest, preferred_element_type=jnp.float32)
    column = jnp.where(mine, local_row, shard_rows)
    placed = (column[:, None] == lax.broadcasted_iota(jnp.int32, (BLOCK, shard_rows), 1)).astype(jnp.float32)
    spread = jnp.dot(increment, placed, precision=highest, preferred_element_type=jnp.float32)
    new_residual = (residual - change) - ridge_weight * spread
    new_coeffs = coeffs + spread
    return (new_residual, new_coeffs)


def solution(mesh):
    dp_parts = (4, mesh.shape["dp"] // 8, 2)
    split = Mesh(mesh.devices.reshape(dp_parts + (mesh.shape["mp"],)), DP + ("mp",))
    placed = (P(DP, None), P("mp", DP), P("mp", DP), P())
    return jax.shard_map(
        on_device,
        mesh=split,
        in_specs=placed,
        out_specs=(P("mp", DP), P("mp", DP)),
        check_vma=False,
    )
```

```python
import jax
import jax.numpy as jnp
from jax import lax
from jax.sharding import Mesh
from jax.sharding import PartitionSpec as P
from jax.experimental import pallas as pl
from jax.experimental.pallas import tpu as pltpu

BLOCK = 512
MOST = 16


ridge_weight = 1.0

DP = ("y", "z", "c")


NB = 128
G = 128


def _dot_nt(a, b):
    return lax.dot_general(a, b, (((1,), (1,)), ((), ())), precision=lax.Precision.HIGHEST,
                           preferred_element_type=jnp.float32)


def _dot_nn(a, b):
    return lax.dot_general(a, b, (((1,), (0,)), ((), ())), precision=lax.Precision.HIGHEST,
                           preferred_element_type=jnp.float32)


def _dot_tn(a, b):
    return lax.dot_general(a, b, (((0,), (0,)), ((), ())), precision=lax.Precision.HIGHEST,
                           preferred_element_type=jnp.float32)


def _solve_kernel(a_ref, r_ref, x_ref, work, up, inv, dg):
    n = a_ref.shape[0]
    blocks = n // NB
    eye = (lax.broadcasted_iota(jnp.int32, (NB, NB), 0) == lax.broadcasted_iota(jnp.int32, (NB, NB), 1)).astype(jnp.float32)
    lane = lax.broadcasted_iota(jnp.int32, (1, NB), 1)
    sub_g = lax.broadcasted_iota(jnp.int32, (G, 1), 0)
    lane_g = lax.broadcasted_iota(jnp.int32, (G, NB), 1)
    for b in range(blocks):
        r0 = b * NB
        src = a_ref if b == 0 else work
        dg[:, :NB] = src[r0:r0 + NB, r0:r0 + NB]
        dg[:, NB:] = eye

        def group(t, carry):
            g0 = pl.multiple_of(t * G, G)
            slab = dg[pl.ds(g0, G), :]
            for j in range(G):
                k = g0 + j
                row = slab[j:j + 1, :]
                c = jnp.sum(jnp.where(lane_g == g0 + sub_g, jnp.broadcast_to(row[:, :NB], (G, NB)), 0.0), axis=1, keepdims=True)
                scale = lax.rsqrt(c[j:j + 1, :])
                u = row * scale
                u_diag = jnp.where(lane >= k, u[:, :NB], 0.0)
                u = jnp.concatenate([u_diag, u[:, NB:]], axis=1)
                u_col = jnp.where(sub_g > j, c * scale, 0.0)
                slab = jnp.where(sub_g == j, u, slab - u_col * u)
            strip = dg[...]
            dg[...] = strip - _dot_tn(slab[:, :NB], slab)
            dg[pl.ds(g0, G), :] = slab
            return carry

        lax.fori_loop(0, NB // G, group, 0)
        up[r0:r0 + NB, r0:r0 + NB] = dg[:, :NB]
        inv[b] = dg[:, NB:]
        if b + 1 < blocks:
            panel = _dot_nn(inv[b], src[r0:r0 + NB, r0 + NB:n])
            up[r0:r0 + NB, r0 + NB:n] = panel
            work[r0 + NB:n, r0 + NB:n] = src[r0 + NB:n, r0 + NB:n] - _dot_tn(panel, panel)
    rhs = r_ref[...]
    z = []
    for b in range(blocks):
        acc = rhs[:, b * NB:(b + 1) * NB]
        for a in range(b):
            acc = acc - _dot_nn(z[a], up[a * NB:(a + 1) * NB, b * NB:(b + 1) * NB])
        z.append(_dot_nt(acc, inv[b]))
    x = [None] * blocks
    for b in reversed(range(blocks)):
        acc = z[b]
        for a in range(b + 1, blocks):
            acc = acc - _dot_nt(x[a], up[b * NB:(b + 1) * NB, a * NB:(a + 1) * NB])
        x[b] = _dot_nn(acc, inv[b])
    x_ref[...] = jnp.concatenate(x, axis=1)


def spd_solve(system, rhs, interpret=False):
    n = system.shape[0]
    return pl.pallas_call(
        _solve_kernel,
        out_shape=jax.ShapeDtypeStruct(rhs.shape, jnp.float32),
        scratch_shapes=[
            pltpu.VMEM((n, n), jnp.float32),
            pltpu.VMEM((n, n), jnp.float32),
            pltpu.VMEM((n // NB, NB, NB), jnp.float32),
            pltpu.VMEM((NB, 2 * NB), jnp.float32),
        ],
        interpret=interpret,
    )(system, rhs)


def on_device(points, residual, coeffs, block_index):
    highest = lax.Precision.HIGHEST
    shard_rows = points.shape[0]
    feature_count = points.shape[1]
    output_rows = residual.shape[0]
    y_count = lax.axis_size("y")
    z_count = lax.axis_size("z")
    c_count = lax.axis_size("c")
    dp_count = y_count * z_count * c_count
    position = (lax.axis_index("y") * z_count + lax.axis_index("z")) * c_count + lax.axis_index("c")
    owner_shard = block_index // shard_rows
    local_row = block_index - owner_shard * shard_rows
    mine = owner_shard == position
    own_squares = jnp.sum(points * points, axis=1)
    own_total = jnp.sum(own_squares)
    same_owner = owner_shard[:, None] == owner_shard[None, :]
    earlier = lax.broadcasted_iota(jnp.int32, (BLOCK, BLOCK), 1) < lax.broadcasted_iota(
        jnp.int32, (BLOCK, BLOCK), 0
    )
    slot_rank = jnp.sum((same_owner & earlier).astype(jnp.int32), axis=1)
    pick = mine[None, :] & (slot_rank[None, :] == lax.broadcasted_iota(jnp.int32, (MOST, BLOCK), 0))
    slot_row = jnp.sum(jnp.where(pick, local_row[None, :], 0), axis=1)
    slot_used = jnp.any(pick, axis=1)
    mp_count = lax.axis_size("mp")
    share = feature_count // mp_count
    slot_points = lax.dynamic_slice_in_dim(points[slot_row], lax.axis_index("mp") * share, share, 1)
    slot_points = jnp.where(slot_used[:, None], slot_points, 0.0)
    slot_resid = jnp.where(slot_used[:, None], residual[:, slot_row].T, 0.0)
    body = jnp.concatenate([slot_points, slot_resid], axis=1)
    extra = jnp.zeros((1, share + output_rows), jnp.float32).at[0, 0].set(own_total)
    packed = jnp.concatenate([body, extra], axis=0)
    per_device = MOST + 1
    gathered = lax.all_gather(packed, "c", axis=0, tiled=True)
    gathered = lax.all_gather(gathered, "z", axis=0, tiled=True)
    gathered = lax.all_gather(gathered, "y", axis=0, tiled=True)
    where_at = owner_shard * per_device + slot_rank
    block_rows = gathered[where_at]
    block_points = lax.all_gather(block_rows[:, :share], "mp", axis=1, tiled=True)
    block_resid = block_rows[:, share:].T
    square_total = jnp.sum(gathered.reshape(dp_count, per_device, -1)[:, MOST, 0])
    mean_sq = square_total / (shard_rows * dp_count)
    block_sq = jnp.sum(block_points * block_points, axis=1)
    inner_block = lax.dot_general(
        block_points,
        block_points,
        (((1,), (1,)), ((), ())),
        precision=highest,
        preferred_element_type=jnp.float32,
    )
    kernel_block = jnp.exp(-(block_sq[:, None] + block_sq[None, :] - 2.0 * inner_block) / mean_sq)
    system = kernel_block + ridge_weight * jnp.eye(BLOCK, dtype=jnp.float32)
    increment = spd_solve(system, block_resid)
    inner = lax.dot_general(
        block_points,
        points,
        (((1,), (1,)), ((), ())),
        precision=highest,
        preferred_element_type=jnp.float32,
    )
    weights = jnp.exp(-(block_sq[:, None] + own_squares[None, :] - 2.0 * inner) / mean_sq)
    change = jnp.dot(increment, weights, precision=highest, preferred_element_type=jnp.float32)
    column = jnp.where(mine, local_row, shard_rows)
    placed = (column[:, None] == lax.broadcasted_iota(jnp.int32, (BLOCK, shard_rows), 1)).astype(jnp.float32)
    spread = jnp.dot(increment, placed, precision=highest, preferred_element_type=jnp.float32)
    new_residual = (residual - change) - ridge_weight * spread
    new_coeffs = coeffs + spread
    return (new_residual, new_coeffs)


def solution(mesh):
    dp_parts = (4, mesh.shape["dp"] // 8, 2)
    split = Mesh(mesh.devices.reshape(dp_parts + (mesh.shape["mp"],)), DP + ("mp",))
    placed = (P(DP, None), P("mp", DP), P("mp", DP), P())
    return jax.shard_map(
        on_device,
        mesh=split,
        in_specs=placed,
        out_specs=(P("mp", DP), P("mp", DP)),
        check_vma=False,
    )
```
